256 devices in a mesh: row: 4 (over y), col: 64 (over z, x, core).
Axes of the slice: x: 4, y: 4, z: 8, core: 2. Of those that a mesh axis runs over, the one named last changes fastest.
Arguments:
- tokens: bfloat16 [32768, 4096], P(('row', 'col')), may hold values from -6 to 6
- expert_ids: int32 [32768, 2], P(('row', 'col')), may hold values from 0 to 63, all different within a row; in each aligned block of 128 rows (0 to 127, 128 to 255, ...) at most 5 rows name the same one
- gate_weights: float32 [32768, 2], P(('row', 'col')), may hold values from 0.1 to 1
- w_gate: bfloat16 [64, 4096, 1536], P('col', None, 'row'), may hold values from -0.09375 to 0.09375
- w_up: bfloat16 [64, 4096, 1536], P('col', None, 'row'), may hold values from -0.09375 to 0.09375
- w_down: bfloat16 [64, 1536, 4096], P('col', None, 'row'), may hold values from -0.15625 to 0.15625
Outputs:
- moe_out: bfloat16 [32768, 4096], P(('row', 'col'))
The draws below stay inside these ranges and needn't reach their ends.
Inputs may be any that keep to these rules, and one draw needn't show every extreme that they name: `expert_ids`: each row names 2 different experts. Among the 128 rows of one device no expert is named by more than 5 rows, and in every draw some expert is named by exactly 5 rows of some device.
All inputs are finite; a program needn't handle non-finite values.
Results may differ from the reference program's by a relative error of at most 0.0058.
Values may be sent and summed in bfloat16 or wider, within the bound.
No kernel may reach another device: no remote copies, remote signals or barrier semaphores. Data moves between devices by JAX's collectives and lax.ppermute only.
A program may use at most 128 MiB of HBM per device.

```python
import math
import jax
import jax.numpy as jnp
import numpy as np
from jax import lax

D = 4096
FF = 1536
TOP = 2
TOK_DEV = 128
EXPERTS = 64
CAP = 5
TOKENS = 32768


def level_of(key, extent, split, low, top_value):
    gain, own = 1.0, jax.random.fold_in(key, 6)
    for dim, parts in split:
        draws = jnp.exp(jax.random.uniform(jax.random.fold_in(own, dim), (parts,), jnp.float32, low / len(split), top_value / len(split)))
        gain = gain * jnp.repeat(draws, extent[dim] // parts).reshape([-1 if axis == dim else 1 for axis in range(len(extent))])
    return gain


def deal_out(stream_key, own, number, rows, count, top, bound, lean):
    ranking = jax.random.permutation(stream_key, count)
    heavy_load, ordinary = load_shares(count, rows * top, bound, lean, True), load_shares(count, rows * top, bound, lean, False)
    places = jnp.arange(count)

    def named(tallies, rotation):
        used = int((tallies > 0).sum())
        fixed = max(1, used // 4)
        shifted = fixed + (places - fixed + rotation * (used - fixed)) % max(1, count - fixed)
        return jnp.zeros((count,), jnp.int32).at[ranking[jnp.where(places < fixed, places, shifted)]].set(jnp.asarray(tallies, jnp.int32))

    tallies = jnp.where(number % 4 == 0, named(heavy_load, number // 4), named(ordinary, number - number // 4 - 1))
    mixed = jax.random.permutation(jax.random.fold_in(own, 3), count)
    donor, sink = mixed[0:count // 2 * 2:2], mixed[1:count // 2 * 2:2]
    margin = jnp.minimum(tallies[donor] - 1, bound - tallies[sink]) // 2
    margin = jnp.where((donor == ranking[0]) | (sink == ranking[0]) | (tallies[sink] == 0), 0, jnp.maximum(margin, 0))
    shifted = jax.random.randint(jax.random.fold_in(own, 4), (count // 2,), 0, 1 << 20) % (margin + 1)
    tallies = tallies.at[donor].add(-shifted).at[sink].add(shifted)
    labels = jnp.searchsorted(jnp.cumsum(tallies), jnp.arange(rows * top), side="right").astype(jnp.int32)
    table = labels.reshape(top, rows).T
    table = table[jax.random.permutation(jax.random.fold_in(own, 1), rows)]
    rotation = jax.random.randint(jax.random.fold_in(own, 2), (rows, 1), 0, top)
    return jnp.take_along_axis(table, (jnp.arange(top)[None, :] + rotation) % top, axis=1)


def load_shares(amount, total, bound, slope, full):
    portions = [(1 << 20) // math.isqrt(grade ** slope) + 1 for grade in range(1, amount + 1)]
    largest = bound if full else min(bound, max(-(-total // amount), total * portions[0] // sum(portions)))
    least = 1 if total - largest >= amount - 1 else 0
    holding, spare = [largest] + [least] * (amount - 1), total - largest - least * (amount - 1)
    while spare > 0:
        movable = [i for i in range(1, amount) if holding[i] < largest] or [i for i in range(1, amount) if holding[i] < bound]
        pool, left = sum([portions[i] for i in movable]), spare
        for i in movable:
            addition = min(bound - holding[i], max(1, left * portions[i] // pool), spare)
            holding[i] = holding[i] + addition
            spare = spare - addition
    return np.array(holding)


def normal_values(key, shape, width, reach, shards=(), kind=jnp.bfloat16):
    values = width * jax.random.normal(key, shape, jnp.float32)
    if shards:
        values = values * level_of(key, shape, shards, -0.22, 0.18)
    return jnp.clip(values, -reach, reach).astype(kind)


def setup_inputs(seed: int = 0) -> dict:
    keys = jax.random.split(jax.random.key(seed), 7)
    tokens = normal_values(keys[0], (TOKENS, D), 1.0, 6.0, ((0, 256),))
    expert_ids_keys = jax.random.split(jax.random.fold_in(keys[1], 1), TOKENS // TOK_DEV)
    expert_ids_turns = jax.random.permutation(jax.random.fold_in(keys[1], 3), TOKENS // TOK_DEV)
    expert_ids = jax.vmap(lambda own, number: deal_out(jax.random.fold_in(keys[1], 2), own, number, TOK_DEV, EXPERTS, TOP, CAP, 2))(expert_ids_keys, expert_ids_turns).reshape((TOKENS, TOP))
    gate_weights = jnp.clip(jnp.exp(math.log(1.0) - 2.3025851 * jax.random.uniform(keys[2], (TOKENS, TOP), jnp.float32) ** level_of(keys[2], (TOKENS, TOP), ((0, 256),), -0.2, 0.2)), 0.1, 1.0)
    w_gate = normal_values(keys[3], (EXPERTS, D, FF), D ** -0.5, 0.09375, ((0, 64), (2, 4)))
    w_up = normal_values(keys[4], (EXPERTS, D, FF), D ** -0.5, 0.09375, ((0, 64), (2, 4)))
    w_down = normal_values(keys[5], (EXPERTS, FF, D), FF ** -0.5, 0.15625, ((0, 64), (2, 4)))
    return dict(tokens=tokens, expert_ids=expert_ids, gate_weights=gate_weights, w_gate=w_gate, w_up=w_up, w_down=w_down)


def reference(tokens, expert_ids, gate_weights, w_gate, w_up, w_down):
    devices = TOKENS // TOK_DEV
    flat_ids = expert_ids.reshape(devices, TOK_DEV * TOP)
    onehot = (flat_ids[:, :, None] == jnp.arange(EXPERTS, dtype=jnp.int32)[None, None, :]).astype(jnp.int32)
    earlier = jnp.cumsum(onehot, axis=1) - onehot
    position = jnp.sum(earlier * onehot, axis=2).astype(jnp.int32)
    slot_ids = (jnp.arange(devices, dtype=jnp.int32)[:, None] * CAP + position).astype(jnp.int32)
    token_of = (jnp.arange(TOKENS * TOP, dtype=jnp.int32) // TOP).astype(jnp.int32)
    shares = gate_weights / jnp.sum(gate_weights, axis=1, keepdims=True)
    row_table = jnp.full((EXPERTS, devices * CAP), TOKENS, jnp.int32)
    row_table = row_table.at[flat_ids.reshape(-1), slot_ids.reshape(-1)].set(token_of)
    weight_table = jnp.zeros((EXPERTS, devices * CAP), jnp.float32)
    weight_table = weight_table.at[flat_ids.reshape(-1), slot_ids.reshape(-1)].set(shares.reshape(-1))
    padded = jnp.concatenate([tokens, jnp.zeros((1, D), tokens.dtype)], axis=0)

    def one_expert(total, inputs):
        row_index, weights, gate_matrix, up_matrix, down_matrix = inputs
        rows = padded[row_index]
        gate_part = jnp.dot(rows, gate_matrix, preferred_element_type=jnp.float32)
        up_part = jnp.dot(rows, up_matrix, preferred_element_type=jnp.float32)
        hidden = (jax.nn.silu(gate_part) * up_part).astype(jnp.bfloat16)
        result = jnp.dot(hidden, down_matrix, preferred_element_type=jnp.float32).astype(jnp.bfloat16)
        total = total.at[row_index].add(weights[:, None] * result.astype(jnp.float32))
        return total, None

    start_total = jnp.zeros((TOKENS + 1, D), jnp.float32)
    total, _ = lax.scan(one_expert, start_total, (row_table, weight_table, w_gate, w_up, w_down))
    return total[:TOKENS].astype(jnp.bfloat16)
```

```python
import jax
import jax.numpy as jnp
from jax import lax
from jax.sharding import PartitionSpec as P

CHUNKS = ((0, 3), (3, 5))


def local(tokens, expert_ids, gate_weights, w_gate, w_up, w_down):
    token_count, top_count = expert_ids.shape
    width = tokens.shape[1]
    unit_count = w_gate.shape[2]
    quarter = w_down.shape[2]
    columns = lax.axis_size("col")
    groups = lax.axis_size("row")
    experts = w_gate.shape[0] * columns
    capacity = max(2, token_count * top_count * 5 // (4 * experts))
    flat_ids = expert_ids.reshape(-1)
    onehot = (flat_ids[:, None] == jnp.arange(experts, dtype=jnp.int32)[None, :]).astype(jnp.int32)
    earlier = jnp.cumsum(onehot, axis=0) - onehot
    position = jnp.sum(earlier * onehot, axis=1)
    slot_ids = (flat_ids * capacity + position).reshape(token_count, top_count)
    shares = gate_weights / jnp.sum(gate_weights, axis=1, keepdims=True)

    all_slots = lax.all_gather(slot_ids, "row", axis=0, tiled=False)
    all_shares = lax.all_gather(shares, "row", axis=0, tiled=False)

    w_down_parts = w_down[0].reshape(groups, unit_count, quarter)
    backs = []
    for lo, hi in CHUNKS:
        span = hi - lo
        wanted = (
            jnp.arange(experts, dtype=jnp.int32)[:, None] * capacity
            + jnp.arange(lo, hi, dtype=jnp.int32)[None, :]
        ).reshape(-1)
        chooser = jnp.any(
            wanted[:, None, None] == slot_ids[None, :, :], axis=2
        ).astype(jnp.bfloat16)
        outgoing = jnp.dot(chooser, tokens, preferred_element_type=jnp.float32).astype(jnp.bfloat16)
        outgoing = outgoing.reshape(columns, span, width)
        arrived = lax.all_to_all(outgoing, "col", split_axis=0, concat_axis=0, tiled=True)
        rows = lax.all_gather(arrived, "row", axis=0, tiled=False)
        rows = rows.reshape(groups * columns * span, width)
        gate_part = jnp.dot(rows, w_gate[0], preferred_element_type=jnp.float32)
        up_part = jnp.dot(rows, w_up[0], preferred_element_type=jnp.float32)
        hidden = (jax.nn.silu(gate_part) * up_part).astype(jnp.bfloat16)
        hidden_all = lax.all_gather(hidden, "row", axis=0, tiled=False)
        result = jnp.einsum(
            "jnu,juf->nf", hidden_all, w_down_parts, preferred_element_type=jnp.float32
        ).astype(jnp.bfloat16)
        result = result.reshape(groups, columns, span, quarter).transpose(1, 0, 2, 3)
        back = lax.all_to_all(result, "col", split_axis=0, concat_axis=0, tiled=True)
        backs.append(back)
    back = jnp.concatenate(backs, axis=2) if len(backs) > 1 else backs[0]
    flat = back.transpose(1, 0, 2, 3).reshape(groups * experts * capacity, quarter)
    index = all_slots + (jnp.arange(groups, dtype=jnp.int32) * (experts * capacity))[:, None, None]
    picked = flat[index.reshape(-1)].reshape(groups, token_count, top_count, quarter)
    combined = jnp.sum(all_shares[:, :, :, None] * picked.astype(jnp.float32), axis=2)
    combined = combined.astype(jnp.bfloat16)
    home = lax.all_to_all(combined, "row", split_axis=0, concat_axis=0, tiled=True)
    return home.transpose(1, 0, 2).reshape(token_count, width)


def solution(mesh):
    placed = (
        P(("row", "col"), None),
        P(("row", "col"), None),
        P(("row", "col"), None),
        P("col", None, "row"),
        P("col", None, "row"),
        P("col", None, "row"),
    )
    return jax.shard_map(
        local, mesh=mesh, in_specs=placed, out_specs=P(("row", "col"), None), check_vma=False
    )
```

```python
import jax
import jax.numpy as jnp
from jax import lax
from jax.sharding import PartitionSpec as P

CHUNKS = ((0, 3), (3, 5))


def local(tokens, expert_ids, gate_weights, w_gate, w_up, w_down):
    token_count, top_count = expert_ids.shape
    width = tokens.shape[1]
    unit_count = w_gate.shape[2]
    quarter = w_down.shape[2]
    columns = lax.axis_size("col")
    groups = lax.axis_size("row")
    experts = w_gate.shape[0] * columns
    capacity = max(2, token_count * top_count * 5 // (4 * experts))
    flat_ids = expert_ids.reshape(-1)
    onehot = (flat_ids[:, None] == jnp.arange(experts, dtype=jnp.int32)[None, :]).astype(jnp.int32)
    earlier = jnp.cumsum(onehot, axis=0) - onehot
    position = jnp.sum(earlier * onehot, axis=1)
    slot_ids = (flat_ids * capacity + position).reshape(token_count, top_count)
    shares = gate_weights / jnp.sum(gate_weights, axis=1, keepdims=True)

    meta = jnp.concatenate([slot_ids.astype(jnp.float32), shares], axis=1)
    meta = lax.all_gather(meta, "row", axis=0, tiled=False)
    all_slots = meta[:, :, :top_count]
    all_shares = meta[:, :, top_count:]

    w_down_parts = w_down[0].reshape(groups, unit_count, quarter)
    combined = jnp.zeros((groups, token_count, quarter), jnp.float32)
    for lo, hi in CHUNKS:
        span = hi - lo
        wanted = (
            jnp.arange(experts, dtype=jnp.int32)[:, None] * capacity
            + jnp.arange(lo, hi, dtype=jnp.int32)[None, :]
        ).reshape(-1)
        chooser = jnp.any(
            wanted[:, None, None] == slot_ids[None, :, :], axis=2
        ).astype(jnp.bfloat16)
        outgoing = jnp.dot(chooser, tokens, preferred_element_type=jnp.float32).astype(jnp.bfloat16)
        outgoing = outgoing.reshape(columns, span, width)
        arrived = lax.all_to_all(outgoing, "col", split_axis=0, concat_axis=0, tiled=True)
        rows = lax.all_gather(arrived, "row", axis=0, tiled=False)
        rows = rows.transpose(2, 0, 1, 3).reshape(span * groups * columns, width)
        gate_part = jnp.dot(rows, w_gate[0], preferred_element_type=jnp.float32)
        up_part = jnp.dot(rows, w_up[0], preferred_element_type=jnp.float32)
        hidden = (jax.nn.silu(gate_part) * up_part).astype(jnp.bfloat16)
        hidden_all = lax.all_gather(hidden, "row", axis=0, tiled=False)
        result = jnp.einsum(
            "jnu,juf->nf", hidden_all, w_down_parts, preferred_element_type=jnp.float32
        ).astype(jnp.bfloat16)
        result = result.reshape(span, groups, columns, quarter).transpose(2, 1, 0, 3)
        back = lax.all_to_all(result, "col", split_axis=0, concat_axis=0, tiled=True)
        match = (all_slots[:, :, :, None] == wanted.astype(jnp.float32)[None, None, None, :])
        weights = jnp.sum(jnp.where(match, all_shares[:, :, :, None], 0.0), axis=2)
        weights = weights.reshape(groups, token_count, experts, span)
        combined = combined + jnp.einsum(
            "rtep,erpf->rtf", weights, back.astype(jnp.float32),
            precision=lax.Precision.HIGHEST, preferred_element_type=jnp.float32,
        )
    combined = combined.astype(jnp.bfloat16)
    home = lax.all_to_all(combined, "row", split_axis=0, concat_axis=0, tiled=True)
    return home.transpose(1, 0, 2).reshape(token_count, width)


def solution(mesh):
    placed = (
        P(("row", "col"), None),
        P(("row", "col"), None),
        P(("row", "col"), None),
        P("col", None, "row"),
        P("col", None, "row"),
        P("col", None, "row"),
    )
    return jax.shard_map(
        local, mesh=mesh, in_specs=placed, out_specs=P(("row", "col"), None), check_vma=False
    )
```

```python
import jax
import jax.numpy as jnp
from jax import lax
from jax.sharding import PartitionSpec as P

CHUNKS = ((0, 2), (2, 5))


def local(tokens, expert_ids, gate_weights, w_gate, w_up, w_down):
    token_count, top_count = expert_ids.shape
    width = tokens.shape[1]
    unit_count = w_gate.shape[2]
    quarter = w_down.shape[2]
    columns = lax.axis_size("col")
    groups = lax.axis_size("row")
    experts = w_gate.shape[0] * columns
    capacity = max(2, token_count * top_count * 5 // (4 * experts))
    flat_ids = expert_ids.reshape(-1)
    onehot = (flat_ids[:, None] == jnp.arange(experts, dtype=jnp.int32)[None, :]).astype(jnp.int32)
    earlier = jnp.cumsum(onehot, axis=0) - onehot
    position = jnp.sum(earlier * onehot, axis=1)
    slot_ids = (flat_ids * capacity + position).reshape(token_count, top_count)
    shares = gate_weights / jnp.sum(gate_weights, axis=1, keepdims=True)

    meta = jnp.concatenate([slot_ids.astype(jnp.float32), shares], axis=1)
    my_row = lax.axis_index("row")
    shifted = [meta]
    for step in range(1, groups):
        pairs = [(i, (i + step) % groups) for i in range(groups)]
        shifted.append(lax.ppermute(meta, "row", pairs))
    order = jnp.stack([shifted[(-s) % groups] for s in range(groups)])
    meta = jnp.roll(order, my_row, axis=0)
    all_slots = meta[:, :, :top_count]
    all_shares = meta[:, :, top_count:]

    w_down_parts = w_down[0].reshape(groups, unit_count, quarter)
    combined = jnp.zeros((groups, token_count, quarter), jnp.float32)
    previous = None
    stages = []
    for lo, hi in CHUNKS:
        span = hi - lo
        wanted = (
            jnp.arange(experts, dtype=jnp.int32)[:, None] * capacity
            + jnp.arange(lo, hi, dtype=jnp.int32)[None, :]
        ).reshape(-1)
        chooser = jnp.any(
            wanted[:, None, None] == slot_ids[None, :, :], axis=2
        ).astype(jnp.bfloat16)
        outgoing = jnp.dot(chooser, tokens, preferred_element_type=jnp.float32).astype(jnp.bfloat16)
        outgoing = outgoing.reshape(columns, span, width)
        if previous is not None:
            outgoing, _ = lax.optimization_barrier((outgoing, previous))
        arrived = lax.all_to_all(outgoing, "col", split_axis=0, concat_axis=0, tiled=True)
        previous = arrived
        rows = lax.all_gather(arrived, "row", axis=0, tiled=False)
        rows = rows.transpose(2, 0, 1, 3).reshape(span * groups * columns, width)
        gate_part = jnp.dot(rows, w_gate[0], preferred_element_type=jnp.float32)
        up_part = jnp.dot(rows, w_up[0], preferred_element_type=jnp.float32)
        hidden = (jax.nn.silu(gate_part) * up_part).astype(jnp.bfloat16)
        stages.append((span, wanted, hidden))

    combined = jnp.zeros((groups, token_count, quarter), jnp.float32)
    for index, (span, wanted, hidden) in enumerate(stages):
        hidden_all = lax.all_gather(hidden, "row", axis=0, tiled=False)
        if index + 1 < len(stages):
            hidden_all, _ = lax.optimization_barrier((hidden_all, stages[index + 1][2]))
        result = jnp.einsum(
            "jnu,juf->nf", hidden_all, w_down_parts, preferred_element_type=jnp.float32
        ).astype(jnp.bfloat16)
        result = result.reshape(span, groups, columns, quarter).transpose(2, 1, 0, 3)
        back = lax.all_to_all(result, "col", split_axis=0, concat_axis=0, tiled=True)
        match = (all_slots[:, :, :, None] == wanted.astype(jnp.float32)[None, None, None, :])
        weights = jnp.sum(jnp.where(match, all_shares[:, :, :, None], 0.0), axis=2)
        weights = weights.reshape(groups, token_count, experts, span)
        combined = combined + jnp.einsum(
            "rtep,erpf->rtf", weights, back.astype(jnp.float32),
            precision=lax.Precision.HIGHEST, preferred_element_type=jnp.float32,
        )
    combined = combined.astype(jnp.bfloat16)
    home = lax.all_to_all(combined, "row", split_axis=0, concat_axis=2, tiled=True)
    return home.reshape(token_count, width)


def solution(mesh):
    placed = (
        P(("row", "col"), None),
        P(("row", "col"), None),
        P(("row", "col"), None),
        P("col", None, "row"),
        P("col", None, "row"),
        P("col", None, "row"),
    )
    return jax.shard_map(
        local, mesh=mesh, in_specs=placed, out_specs=P(("row", "col"), None), check_vma=False
    )
```

```python
import jax
import jax.numpy as jnp
from jax import lax
from jax.sharding import PartitionSpec as P

CHUNKS = ((0, 1), (1, 3), (3, 5))


def local(tokens, expert_ids, gate_weights, w_gate, w_up, w_down):
    token_count, top_count = expert_ids.shape
    width = tokens.shape[1]
    unit_count = w_gate.shape[2]
    quarter = w_down.shape[2]
    columns = lax.axis_size("col")
    groups = lax.axis_size("row")
    experts = w_gate.shape[0] * columns
    capacity = max(2, token_count * top_count * 5 // (4 * experts))
    flat_ids = expert_ids.reshape(-1)
    onehot = (flat_ids[:, None] == jnp.arange(experts, dtype=jnp.int32)[None, :]).astype(jnp.int32)
    earlier = jnp.cumsum(onehot, axis=0) - onehot
    position = jnp.sum(earlier * onehot, axis=1)
    slot_ids = (flat_ids * capacity + position).reshape(token_count, top_count)
    shares = gate_weights / jnp.sum(gate_weights, axis=1, keepdims=True)

    meta = jnp.concatenate([slot_ids.astype(jnp.float32), shares], axis=1)
    my_row = lax.axis_index("row")
    shifted = [meta]
    for step in range(1, groups):
        pairs = [(i, (i + step) % groups) for i in range(groups)]
        shifted.append(lax.ppermute(meta, "row", pairs))
    order = jnp.stack([shifted[(-s) % groups] for s in range(groups)])
    meta = jnp.roll(order, my_row, axis=0)

    w_down_parts = w_down[0].reshape(groups, unit_count, quarter)
    all_slots = meta[:, :, :top_count]
    all_shares = meta[:, :, top_count:]
    combined = jnp.zeros((groups, token_count, quarter), jnp.float32)
    previous = None
    stages = []
    for lo, hi in CHUNKS:
        span = hi - lo
        wanted = (
            jnp.arange(experts, dtype=jnp.int32)[:, None] * capacity
            + jnp.arange(lo, hi, dtype=jnp.int32)[None, :]
        ).reshape(-1)
        chooser = jnp.any(
            wanted[:, None, None] == slot_ids[None, :, :], axis=2
        ).astype(jnp.bfloat16)
        outgoing = jnp.dot(chooser, tokens, preferred_element_type=jnp.float32).astype(jnp.bfloat16)
        outgoing = outgoing.reshape(columns, span, width)
        if previous is not None:
            outgoing, _, meta = lax.optimization_barrier((outgoing, previous, meta))
        arrived = lax.all_to_all(outgoing, "col", split_axis=0, concat_axis=0, tiled=True)
        previous = arrived
        rows = lax.all_gather(arrived, "row", axis=0, tiled=False)
        rows = rows.transpose(2, 0, 1, 3).reshape(span * groups * columns, width)
        gate_part = jnp.dot(rows, w_gate[0], preferred_element_type=jnp.float32)
        up_part = jnp.dot(rows, w_up[0], preferred_element_type=jnp.float32)
        hidden = (jax.nn.silu(gate_part) * up_part).astype(jnp.bfloat16)
        stages.append((span, wanted, hidden))

    all_slots = meta[:, :, :top_count]
    all_shares = meta[:, :, top_count:]
    combined = jnp.zeros((groups, token_count, quarter), jnp.float32)
    for index, (span, wanted, hidden) in enumerate(stages):
        hidden_all = lax.all_gather(hidden, "row", axis=0, tiled=False)
        if index + 1 < len(stages):
            hidden_all, _ = lax.optimization_barrier((hidden_all, stages[index + 1][2]))
        result = jnp.einsum(
            "jnu,juf->nf", hidden_all, w_down_parts, preferred_element_type=jnp.float32
        ).astype(jnp.bfloat16)
        result = result.reshape(span, groups, columns, quarter).transpose(2, 1, 0, 3)
        back = lax.all_to_all(result, "col", split_axis=0, concat_axis=0, tiled=True)
        match = (all_slots[:, :, :, None] == wanted.astype(jnp.float32)[None, None, None, :])
        weights = jnp.sum(jnp.where(match, all_shares[:, :, :, None], 0.0), axis=2)
        weights = weights.reshape(groups, token_count, experts, span)
        combined = combined + jnp.einsum(
            "rtep,erpf->rtf", weights, back.astype(jnp.float32),
            precision=lax.Precision.HIGHEST, preferred_element_type=jnp.float32,
        )
    combined = combined.astype(jnp.bfloat16)
    home = lax.all_to_all(combined, "row", split_axis=0, concat_axis=2, tiled=True)
    return home.reshape(token_count, width)


def solution(mesh):
    placed = (
        P(("row", "col"), None),
        P(("row", "col"), None),
        P(("row", "col"), None),
        P("col", None, "row"),
        P("col", None, "row"),
        P("col", None, "row"),
    )
    return jax.shard_map(
        local, mesh=mesh, in_specs=placed, out_specs=P(("row", "col"), None), check_vma=False
    )
```

```python
import jax
import jax.numpy as jnp
from jax import lax
from jax.sharding import PartitionSpec as P

CHUNKS = ((0, 2), (2, 5))


def local(tokens, expert_ids, gate_weights, w_gate, w_up, w_down):
    token_count, top_count = expert_ids.shape
    width = tokens.shape[1]
    unit_count = w_gate.shape[2]
    quarter = w_down.shape[2]
    columns = lax.axis_size("col")
    groups = lax.axis_size("row")
    experts = w_gate.shape[0] * columns
    capacity = max(2, token_count * top_count * 5 // (4 * experts))
    flat_ids = expert_ids.reshape(-1)
    onehot = (flat_ids[:, None] == jnp.arange(experts, dtype=jnp.int32)[None, :]).astype(jnp.int32)
    earlier = jnp.cumsum(onehot, axis=0) - onehot
    position = jnp.sum(earlier * onehot, axis=1)
    slot_ids = (flat_ids * capacity + position).reshape(token_count, top_count)
    shares = gate_weights / jnp.sum(gate_weights, axis=1, keepdims=True)

    meta = jnp.concatenate([slot_ids.astype(jnp.float32), shares], axis=1)
    my_row = lax.axis_index("row")
    shifted = [meta]
    for step in range(1, groups):
        pairs = [(i, (i + step) % groups) for i in range(groups)]
        shifted.append(lax.ppermute(meta, "row", pairs))
    order = jnp.stack([shifted[(-s) % groups] for s in range(groups)])
    meta = jnp.roll(order, my_row, axis=0)
    all_slots = meta[:, :, :top_count]
    all_shares = meta[:, :, top_count:]

    w_down_parts = w_down[0].reshape(groups, unit_count, quarter)
    combined = jnp.zeros((groups, token_count, quarter), jnp.float32)
    previous = None
    stages = []
    for lo, hi in CHUNKS:
        span = hi - lo
        wanted = (
            jnp.arange(experts, dtype=jnp.int32)[:, None] * capacity
            + jnp.arange(lo, hi, dtype=jnp.int32)[None, :]
        ).reshape(-1)
        chooser = jnp.any(
            wanted[:, None, None] == slot_ids[None, :, :], axis=2
        ).astype(jnp.bfloat16)
        outgoing = jnp.dot(chooser, tokens, preferred_element_type=jnp.float32).astype(jnp.bfloat16)
        outgoing = outgoing.reshape(columns, span * width // 128, 128)
        if previous is not None:
            outgoing, _ = lax.optimization_barrier((outgoing, previous))
        arrived = lax.all_to_all(outgoing, "col", split_axis=0, concat_axis=0, tiled=True)
        previous = arrived
        arrived = arrived.reshape(columns, span, width)
        rows = lax.all_gather(arrived, "row", axis=0, tiled=False)
        rows = rows.transpose(2, 0, 1, 3).reshape(span * groups * columns, width)
        gate_part = jnp.dot(rows, w_gate[0], preferred_element_type=jnp.float32)
        up_part = jnp.dot(rows, w_up[0], preferred_element_type=jnp.float32)
        hidden = (jax.nn.silu(gate_part) * up_part).astype(jnp.bfloat16)
        stages.append((span, wanted, hidden))

    combined = jnp.zeros((groups, token_count, quarter), jnp.float32)
    for index, (span, wanted, hidden) in enumerate(stages):
        hidden_all = lax.all_gather(hidden, "row", axis=0, tiled=False)
        if index + 1 < len(stages):
            hidden_all, _ = lax.optimization_barrier((hidden_all, stages[index + 1][2]))
        result = jnp.einsum(
            "jnu,juf->nf", hidden_all, w_down_parts, preferred_element_type=jnp.float32
        ).astype(jnp.bfloat16)
        result = result.reshape(span, groups, columns, quarter).transpose(2, 1, 0, 3)
        result = result.reshape(columns, groups * span * quarter // 128, 128)
        back = lax.all_to_all(result, "col", split_axis=0, concat_axis=0, tiled=True)
        back = back.reshape(experts, groups, span, quarter)
        match = (all_slots[:, :, :, None] == wanted.astype(jnp.float32)[None, None, None, :])
        weights = jnp.sum(jnp.where(match, all_shares[:, :, :, None], 0.0), axis=2)
        weights = weights.reshape(groups, token_count, experts, span)
        combined = combined + jnp.einsum(
            "rtep,erpf->rtf", weights, back.astype(jnp.float32),
            precision=lax.Precision.HIGHEST, preferred_element_type=jnp.float32,
        )
    combined = combined.astype(jnp.bfloat16)
    home = lax.all_to_all(combined, "row", split_axis=0, concat_axis=2, tiled=True)
    return home.reshape(token_count, width)


def solution(mesh):
    placed = (
        P(("row", "col"), None),
        P(("row", "col"), None),
        P(("row", "col"), None),
        P("col", None, "row"),
        P("col", None, "row"),
        P("col", None, "row"),
    )
    return jax.shard_map(
        local, mesh=mesh, in_specs=placed, out_specs=P(("row", "col"), None), check_vma=False
    )
```

```python
import jax
import jax.numpy as jnp
from jax import lax
from jax.sharding import PartitionSpec as P

CHUNKS = ((0, 2), (2, 5))


def local(tokens, expert_ids, gate_weights, w_gate, w_up, w_down):
    token_count, top_count = expert_ids.shape
    width = tokens.shape[1]
    unit_count = w_gate.shape[2]
    quarter = w_down.shape[2]
    columns = lax.axis_size("col")
    groups = lax.axis_size("row")
    experts = w_gate.shape[0] * columns
    capacity = max(2, token_count * top_count * 5 // (4 * experts))
    flat_ids = expert_ids.reshape(-1)
    onehot = (flat_ids[:, None] == jnp.arange(experts, dtype=jnp.int32)[None, :]).astype(jnp.int32)
    earlier = jnp.cumsum(onehot, axis=0) - onehot
    position = jnp.sum(earlier * onehot, axis=1)
    slot_ids = (flat_ids * capacity + position).reshape(token_count, top_count)
    shares = gate_weights / jnp.sum(gate_weights, axis=1, keepdims=True)

    meta = jnp.concatenate([slot_ids.astype(jnp.float32), shares], axis=1)
    my_row = lax.axis_index("row")
    shifted = [meta]
    for step in range(1, groups):
        pairs = [(i, (i + step) % groups) for i in range(groups)]
        shifted.append(lax.ppermute(meta, "row", pairs))
    order = jnp.stack([shifted[(-s) % groups] for s in range(groups)])
    meta = jnp.roll(order, my_row, axis=0)
    all_slots = meta[:, :, :top_count]
    all_shares = meta[:, :, top_count:]

    w_down_parts = w_down[0].reshape(groups, unit_count, quarter)
    combined = jnp.zeros((groups, token_count, quarter), jnp.float32)
    previous = None
    stages = []
    for lo, hi in CHUNKS:
        span = hi - lo
        wanted = (
            jnp.arange(experts, dtype=jnp.int32)[:, None] * capacity
            + jnp.arange(lo, hi, dtype=jnp.int32)[None, :]
        ).reshape(-1)
        chooser = jnp.any(
            wanted[:, None, None] == slot_ids[None, :, :], axis=2
        ).astype(jnp.bfloat16)
        outgoing = jnp.dot(chooser, tokens, preferred_element_type=jnp.float32).astype(jnp.bfloat16)
        outgoing = outgoing.reshape(columns, span * width // 128, 128)
        if previous is not None:
            outgoing, _ = lax.optimization_barrier((outgoing, previous))
        arrived = lax.all_to_all(outgoing, "col", split_axis=0, concat_axis=0, tiled=True)
        previous = arrived
        rows = lax.all_gather(arrived, "row", axis=0, tiled=False)
        rows = rows.reshape(groups * columns, span, width // 128, 128)
        gate_w = w_gate[0].reshape(width // 128, 128, unit_count)
        up_w = w_up[0].reshape(width // 128, 128, unit_count)
        gate_part = jnp.einsum("npak,aku->npu", rows, gate_w, preferred_element_type=jnp.float32)
        up_part = jnp.einsum("npak,aku->npu", rows, up_w, preferred_element_type=jnp.float32)
        gate_part = gate_part.reshape(groups * columns * span, unit_count)
        up_part = up_part.reshape(groups * columns * span, unit_count)
        hidden = (jax.nn.silu(gate_part) * up_part).astype(jnp.bfloat16)
        stages.append((span, wanted, hidden))

    combined = jnp.zeros((groups, token_count, quarter), jnp.float32)
    for index, (span, wanted, hidden) in enumerate(stages):
        hidden_all = lax.all_gather(hidden, "row", axis=0, tiled=False)
        if index + 1 < len(stages):
            hidden_all, _ = lax.optimization_barrier((hidden_all, stages[index + 1][2]))
        result = jnp.einsum(
            "jnu,juf->nf", hidden_all, w_down_parts, preferred_element_type=jnp.float32
        ).astype(jnp.bfloat16)
        result = result.reshape(groups, columns, span, quarter).transpose(1, 0, 2, 3)
        back = lax.all_to_all(result, "col", split_axis=0, concat_axis=0, tiled=True)
        match = (all_slots[:, :, :, None] == wanted.astype(jnp.float32)[None, None, None, :])
        weights = jnp.sum(jnp.where(match, all_shares[:, :, :, None], 0.0), axis=2)
        weights = weights.reshape(groups, token_count, experts, span)
        combined = combined + jnp.einsum(
            "rtep,erpf->rtf", weights, back.astype(jnp.float32),
            precision=lax.Precision.HIGHEST, preferred_element_type=jnp.float32,
        )
    combined = combined.astype(jnp.bfloat16)
    home = lax.all_to_all(combined, "row", split_axis=0, concat_axis=2, tiled=True)
    return home.reshape(token_count, width)


def solution(mesh):
    placed = (
        P(("row", "col"), None),
        P(("row", "col"), None),
        P(("row", "col"), None),
        P("col", None, "row"),
        P("col", None, "row"),
        P("col", None, "row"),
    )
    return jax.shard_map(
        local, mesh=mesh, in_specs=placed, out_specs=P(("row", "col"), None), check_vma=False
    )
```

```python
import jax
import jax.numpy as jnp
from jax import lax
from jax.sharding import PartitionSpec as P

CHUNKS = ((0, 2), (2, 5))


def local(tokens, expert_ids, gate_weights, w_gate, w_up, w_down):
    token_count, top_count = expert_ids.shape
    width = tokens.shape[1]
    unit_count = w_gate.shape[2]
    quarter = w_down.shape[2]
    columns = lax.axis_size("col")
    groups = lax.axis_size("row")
    experts = w_gate.shape[0] * columns
    capacity = max(2, token_count * top_count * 5 // (4 * experts))
    flat_ids = expert_ids.reshape(-1)
    onehot = (flat_ids[:, None] == jnp.arange(experts, dtype=jnp.int32)[None, :]).astype(jnp.int32)
    earlier = jnp.cumsum(onehot, axis=0) - onehot
    position = jnp.sum(earlier * onehot, axis=1)
    slot_ids = (flat_ids * capacity + position).reshape(token_count, top_count)
    shares = gate_weights / jnp.sum(gate_weights, axis=1, keepdims=True)

    meta = jnp.concatenate([slot_ids.astype(jnp.float32), shares], axis=1)
    my_row = lax.axis_index("row")
    shifted = [meta]
    for step in range(1, groups):
        pairs = [(i, (i + step) % groups) for i in range(groups)]
        shifted.append(lax.ppermute(meta, "row", pairs))
    order = jnp.stack([shifted[(-s) % groups] for s in range(groups)])
    meta = jnp.roll(order, my_row, axis=0)

    w_down_parts = w_down[0].reshape(groups, unit_count, quarter)
    previous = None
    stages = []
    for lo, hi in CHUNKS:
        span = hi - lo
        wanted = (
            jnp.arange(experts, dtype=jnp.int32)[:, None] * capacity
            + jnp.arange(lo, hi, dtype=jnp.int32)[None, :]
        ).reshape(-1)
        chooser = jnp.any(
            wanted[:, None, None] == slot_ids[None, :, :], axis=2
        ).astype(jnp.bfloat16)
        outgoing = jnp.dot(chooser, tokens, preferred_element_type=jnp.float32).astype(jnp.bfloat16)
        outgoing = outgoing.reshape(columns, span * width // 128, 128)
        if previous is not None:
            outgoing, _, meta = lax.optimization_barrier((outgoing, previous, meta))
        arrived = lax.all_to_all(outgoing, "col", split_axis=0, concat_axis=0, tiled=True)
        previous = arrived
        rows = lax.all_gather(arrived, "row", axis=0, tiled=False)
        rows = rows.reshape(groups * columns, span, width // 128, 128)
        gate_w = w_gate[0].reshape(width // 128, 128, unit_count)
        up_w = w_up[0].reshape(width // 128, 128, unit_count)
        gate_part = jnp.einsum("npak,aku->npu", rows, gate_w, preferred_element_type=jnp.float32)
        up_part = jnp.einsum("npak,aku->npu", rows, up_w, preferred_element_type=jnp.float32)
        gate_part = gate_part.reshape(groups * columns * span, unit_count)
        up_part = up_part.reshape(groups * columns * span, unit_count)
        hidden = (jax.nn.silu(gate_part) * up_part).astype(jnp.bfloat16)
        stages.append((span, wanted, hidden))

    all_slots = meta[:, :, :top_count]
    all_shares = meta[:, :, top_count:]
    joined = jnp.concatenate(
        [h.reshape(groups, columns, span, unit_count).transpose(1, 0, 2, 3) for span, _, h in stages],
        axis=2,
    ).reshape(columns * groups * capacity, unit_count)
    hidden_all = lax.all_gather(joined, "row", axis=0, tiled=False)
    result = jnp.einsum(
        "jnu,juf->nf", hidden_all, w_down_parts, preferred_element_type=jnp.float32
    ).astype(jnp.bfloat16)
    result = result.reshape(columns, groups, capacity, quarter)
    back = lax.all_to_all(result, "col", split_axis=0, concat_axis=0, tiled=True)
    wanted = jnp.arange(experts * capacity, dtype=jnp.float32)
    match = (all_slots[:, :, :, None] == wanted[None, None, None, :])
    weights = jnp.sum(jnp.where(match, all_shares[:, :, :, None], 0.0), axis=2)
    weights = weights.reshape(groups, token_count, experts, capacity)
    combined = jnp.einsum(
        "rtep,erpf->rtf", weights, back.astype(jnp.float32),
        precision=lax.Precision.HIGHEST, preferred_element_type=jnp.float32,
    )
    combined = combined.astype(jnp.bfloat16)
    home = lax.all_to_all(combined, "row", split_axis=0, concat_axis=2, tiled=True)
    return home.reshape(token_count, width)


def solution(mesh):
    placed = (
        P(("row", "col"), None),
        P(("row", "col"), None),
        P(("row", "col"), None),
        P("col", None, "row"),
        P("col", None, "row"),
        P("col", None, "row"),
    )
    return jax.shard_map(
        local, mesh=mesh, in_specs=placed, out_specs=P(("row", "col"), None), check_vma=False
    )
```

```python
import jax
import jax.numpy as jnp
from jax import lax
from jax.sharding import PartitionSpec as P

CHUNKS = ((0, 2), (2, 5))


def local(tokens, expert_ids, gate_weights, w_gate, w_up, w_down):
    token_count, top_count = expert_ids.shape
    width = tokens.shape[1]
    unit_count = w_gate.shape[2]
    quarter = w_down.shape[2]
    columns = lax.axis_size("col")
    groups = lax.axis_size("row")
    experts = w_gate.shape[0] * columns
    capacity = max(2, token_count * top_count * 5 // (4 * experts))
    flat_ids = expert_ids.reshape(-1)
    onehot = (flat_ids[:, None] == jnp.arange(experts, dtype=jnp.int32)[None, :]).astype(jnp.int32)
    earlier = jnp.cumsum(onehot, axis=0) - onehot
    position = jnp.sum(earlier * onehot, axis=1)
    slot_ids = (flat_ids * capacity + position).reshape(token_count, top_count)
    shares = gate_weights / jnp.sum(gate_weights, axis=1, keepdims=True)

    meta = jnp.concatenate([slot_ids.astype(jnp.float32), shares], axis=1)
    my_row = lax.axis_index("row")
    shifted = [meta]
    for step in range(1, groups):
        pairs = [(i, (i + step) % groups) for i in range(groups)]
        shifted.append(lax.ppermute(meta, "row", pairs))
    order = jnp.stack([shifted[(-s) % groups] for s in range(groups)])
    meta = jnp.roll(order, my_row, axis=0)

    w_down_parts = w_down[0].reshape(groups, unit_count, quarter)
    combined = jnp.zeros((groups, token_count, quarter), jnp.float32)
    previous = None
    stages = []
    for lo, hi in CHUNKS:
        span = hi - lo
        wanted = (
            jnp.arange(experts, dtype=jnp.int32)[:, None] * capacity
            + jnp.arange(lo, hi, dtype=jnp.int32)[None, :]
        ).reshape(-1)
        chooser = jnp.any(
            wanted[:, None, None] == slot_ids[None, :, :], axis=2
        ).astype(jnp.bfloat16)
        outgoing = jnp.dot(chooser, tokens, preferred_element_type=jnp.float32).astype(jnp.bfloat16)
        outgoing = outgoing.reshape(columns, span * width // 128, 128)
        if previous is not None:
            outgoing, _, meta = lax.optimization_barrier((outgoing, previous, meta))
        arrived = lax.all_to_all(outgoing, "col", split_axis=0, concat_axis=0, tiled=True)
        previous = arrived
        rows = lax.all_gather(arrived, "row", axis=0, tiled=False)
        rows = rows.reshape(groups * columns, span, width // 128, 128)
        gate_w = w_gate[0].reshape(width // 128, 128, unit_count)
        up_w = w_up[0].reshape(width // 128, 128, unit_count)
        gate_part = jnp.einsum("npak,aku->npu", rows, gate_w, preferred_element_type=jnp.float32)
        up_part = jnp.einsum("npak,aku->npu", rows, up_w, preferred_element_type=jnp.float32)
        gate_part = gate_part.reshape(groups * columns * span, unit_count)
        up_part = up_part.reshape(groups * columns * span, unit_count)
        hidden = (jax.nn.silu(gate_part) * up_part).astype(jnp.bfloat16)
        stages.append((span, wanted, hidden))

    all_slots = meta[:, :, :top_count]
    all_shares = meta[:, :, top_count:]
    down_blocks = [
        lax.dynamic_index_in_dim(w_down_parts, (my_row - step) % groups, axis=0, keepdims=False)
        for step in range(groups)
    ]
    combined = jnp.zeros((groups, token_count, quarter), jnp.float32)
    for index, (span, wanted, hidden) in enumerate(stages):
        total = jnp.dot(hidden, down_blocks[0], preferred_element_type=jnp.float32)
        for step in range(1, groups):
            pairs = [(i, (i + step) % groups) for i in range(groups)]
            moved = lax.ppermute(hidden, "row", pairs)
            total = total + jnp.dot(moved, down_blocks[step], preferred_element_type=jnp.float32)
        result = total.astype(jnp.bfloat16)
        result = result.reshape(groups, columns, span, quarter).transpose(1, 0, 2, 3)
        back = lax.all_to_all(result, "col", split_axis=0, concat_axis=0, tiled=True)
        match = (all_slots[:, :, :, None] == wanted.astype(jnp.float32)[None, None, None, :])
        weights = jnp.sum(jnp.where(match, all_shares[:, :, :, None], 0.0), axis=2)
        weights = weights.reshape(groups, token_count, experts, span)
        combined = combined + jnp.einsum(
            "rtep,erpf->rtf", weights, back.astype(jnp.float32),
            precision=lax.Precision.HIGHEST, preferred_element_type=jnp.float32,
        )
    combined = combined.astype(jnp.bfloat16)
    home = lax.all_to_all(combined, "row", split_axis=0, concat_axis=2, tiled=True)
    return home.reshape(token_count, width)


def solution(mesh):
    placed = (
        P(("row", "col"), None),
        P(("row", "col"), None),
        P(("row", "col"), None),
        P("col", None, "row"),
        P("col", None, "row"),
        P("col", None, "row"),
    )
    return jax.shard_map(
        local, mesh=mesh, in_specs=placed, out_specs=P(("row", "col"), None), check_vma=False
    )
```

```python
import jax
import jax.numpy as jnp
from jax import lax
from jax.sharding import PartitionSpec as P

CHUNKS = ((0, 3), (3, 5))


def local(tokens, expert_ids, gate_weights, w_gate, w_up, w_down):
    token_count, top_count = expert_ids.shape
    width = tokens.shape[1]
    unit_count = w_gate.shape[2]
    quarter = w_down.shape[2]
    columns = lax.axis_size("col")
    groups = lax.axis_size("row")
    experts = w_gate.shape[0] * columns
    capacity = max(2, token_count * top_count * 5 // (4 * experts))
    flat_ids = expert_ids.reshape(-1)
    onehot = (flat_ids[:, None] == jnp.arange(experts, dtype=jnp.int32)[None, :]).astype(jnp.int32)
    earlier = jnp.cumsum(onehot, axis=0) - onehot
    position = jnp.sum(earlier * onehot, axis=1)
    slot_ids = (flat_ids * capacity + position).reshape(token_count, top_count)
    shares = gate_weights / jnp.sum(gate_weights, axis=1, keepdims=True)

    meta = jnp.concatenate([slot_ids.astype(jnp.float32), shares], axis=1)
    my_row = lax.axis_index("row")
    shifted = [meta]
    for step in range(1, groups):
        pairs = [(i, (i + step) % groups) for i in range(groups)]
        shifted.append(lax.ppermute(meta, "row", pairs))
    order = jnp.stack([shifted[(-s) % groups] for s in range(groups)])
    meta = jnp.roll(order, my_row, axis=0)

    w_down_parts = w_down[0].reshape(groups, unit_count, quarter)
    combined = jnp.zeros((groups, token_count, quarter), jnp.float32)
    previous = None
    stages = []
    for lo, hi in CHUNKS:
        span = hi - lo
        wanted = (
            jnp.arange(experts, dtype=jnp.int32)[:, None] * capacity
            + jnp.arange(lo, hi, dtype=jnp.int32)[None, :]
        ).reshape(-1)
        chooser = jnp.any(
            wanted[:, None, None] == slot_ids[None, :, :], axis=2
        ).astype(jnp.bfloat16)
        outgoing = jnp.dot(chooser, tokens, preferred_element_type=jnp.float32).astype(jnp.bfloat16)
        outgoing = outgoing.reshape(columns, span * width // 128, 128)
        if previous is not None:
            outgoing, _, meta = lax.optimization_barrier((outgoing, previous, meta))
        arrived = lax.all_to_all(outgoing, "col", split_axis=0, concat_axis=0, tiled=True)
        previous = arrived
        rows = lax.all_gather(arrived, "row", axis=0, tiled=False)
        rows = rows.reshape(groups * columns, span, width // 128, 128)
        gate_w = w_gate[0].reshape(width // 128, 128, unit_count)
        up_w = w_up[0].reshape(width // 128, 128, unit_count)
        gate_part = jnp.einsum("npak,aku->npu", rows, gate_w, preferred_element_type=jnp.float32)
        up_part = jnp.einsum("npak,aku->npu", rows, up_w, preferred_element_type=jnp.float32)
        gate_part = gate_part.reshape(groups * columns * span, unit_count)
        up_part = up_part.reshape(groups * columns * span, unit_count)
        hidden = (jax.nn.silu(gate_part) * up_part).astype(jnp.bfloat16)
        stages.append((span, wanted, hidden))

    all_slots = meta[:, :, :top_count]
    all_shares = meta[:, :, top_count:]
    down_blocks = [
        lax.dynamic_index_in_dim(w_down_parts, (my_row - step) % groups, axis=0, keepdims=False)
        for step in range(groups)
    ]
    combined = jnp.zeros((groups, token_count, quarter), jnp.float32)
    for index, (span, wanted, hidden) in enumerate(stages):
        total = jnp.dot(hidden, down_blocks[0], preferred_element_type=jnp.float32)
        for step in range(1, groups):
            pairs = [(i, (i + step) % groups) for i in range(groups)]
            moved = lax.ppermute(hidden, "row", pairs)
            total = total + jnp.dot(moved, down_blocks[step], preferred_element_type=jnp.float32)
        result = total.astype(jnp.bfloat16)
        result = result.reshape(groups, columns, span, quarter).transpose(1, 0, 2, 3)
        back = lax.all_to_all(result, "col", split_axis=0, concat_axis=0, tiled=True)
        match = (all_slots[:, :, :, None] == wanted.astype(jnp.float32)[None, None, None, :])
        weights = jnp.sum(jnp.where(match, all_shares[:, :, :, None], 0.0), axis=2)
        weights = weights.reshape(groups, token_count, experts, span)
        combined = combined + jnp.einsum(
            "rtep,erpf->rtf", weights, back.astype(jnp.float32),
            precision=lax.Precision.HIGHEST, preferred_element_type=jnp.float32,
        )
    combined = combined.astype(jnp.bfloat16)
    home = lax.all_to_all(combined, "row", split_axis=0, concat_axis=2, tiled=True)
    return home.reshape(token_count, width)


def solution(mesh):
    placed = (
        P(("row", "col"), None),
        P(("row", "col"), None),
        P(("row", "col"), None),
        P("col", None, "row"),
        P("col", None, "row"),
        P("col", None, "row"),
    )
    return jax.shard_map(
        local, mesh=mesh, in_specs=placed, out_specs=P(("row", "col"), None), check_vma=False
    )
```

```python
import jax
import jax.numpy as jnp
from jax import lax
from jax.sharding import PartitionSpec as P

CHUNKS = ((0, 2), (2, 4), (4, 5))


def local(tokens, expert_ids, gate_weights, w_gate, w_up, w_down):
    token_count, top_count = expert_ids.shape
    width = tokens.shape[1]
    unit_count = w_gate.shape[2]
    quarter = w_down.shape[2]
    columns = lax.axis_size("col")
    groups = lax.axis_size("row")
    experts = w_gate.shape[0] * columns
    capacity = max(2, token_count * top_count * 5 // (4 * experts))
    flat_ids = expert_ids.reshape(-1)
    onehot = (flat_ids[:, None] == jnp.arange(experts, dtype=jnp.int32)[None, :]).astype(jnp.int32)
    earlier = jnp.cumsum(onehot, axis=0) - onehot
    position = jnp.sum(earlier * onehot, axis=1)
    slot_ids = (flat_ids * capacity + position).reshape(token_count, top_count)
    shares = gate_weights / jnp.sum(gate_weights, axis=1, keepdims=True)

    meta = jnp.concatenate([slot_ids.astype(jnp.float32), shares], axis=1)
    my_row = lax.axis_index("row")
    shifted = [meta]
    for step in range(1, groups):
        pairs = [(i, (i + step) % groups) for i in range(groups)]
        shifted.append(lax.ppermute(meta, "row", pairs))
    order = jnp.stack([shifted[(-s) % groups] for s in range(groups)])
    meta = jnp.roll(order, my_row, axis=0)

    w_down_parts = w_down[0].reshape(groups, unit_count, quarter)
    combined = jnp.zeros((groups, token_count, quarter), jnp.float32)
    previous = None
    stages = []
    for lo, hi in CHUNKS:
        span = hi - lo
        wanted = (
            jnp.arange(experts, dtype=jnp.int32)[:, None] * capacity
            + jnp.arange(lo, hi, dtype=jnp.int32)[None, :]
        ).reshape(-1)
        chooser = jnp.any(
            wanted[:, None, None] == slot_ids[None, :, :], axis=2
        ).astype(jnp.bfloat16)
        outgoing = jnp.dot(chooser, tokens, preferred_element_type=jnp.float32).astype(jnp.bfloat16)
        outgoing = outgoing.reshape(columns, span * width // 128, 128)
        if previous is not None:
            outgoing, _, meta = lax.optimization_barrier((outgoing, previous, meta))
        arrived = lax.all_to_all(outgoing, "col", split_axis=0, concat_axis=0, tiled=True)
        previous = arrived
        rows = lax.all_gather(arrived, "row", axis=0, tiled=False)
        rows = rows.reshape(groups * columns, span, width // 128, 128)
        gate_w = w_gate[0].reshape(width // 128, 128, unit_count)
        up_w = w_up[0].reshape(width // 128, 128, unit_count)
        gate_part = jnp.einsum("npak,aku->npu", rows, gate_w, preferred_element_type=jnp.float32)
        up_part = jnp.einsum("npak,aku->npu", rows, up_w, preferred_element_type=jnp.float32)
        gate_part = gate_part.reshape(groups * columns * span, unit_count)
        up_part = up_part.reshape(groups * columns * span, unit_count)
        hidden = (jax.nn.silu(gate_part) * up_part).astype(jnp.bfloat16)
        stages.append((span, wanted, hidden))

    all_slots = meta[:, :, :top_count]
    all_shares = meta[:, :, top_count:]
    down_blocks = [
        lax.dynamic_index_in_dim(w_down_parts, (my_row - step) % groups, axis=0, keepdims=False)
        for step in range(groups)
    ]
    combined = jnp.zeros((groups, token_count, quarter), jnp.float32)
    for index, (span, wanted, hidden) in enumerate(stages):
        total = jnp.dot(hidden, down_blocks[0], preferred_element_type=jnp.float32)
        for step in range(1, groups):
            pairs = [(i, (i + step) % groups) for i in range(groups)]
            moved = lax.ppermute(hidden, "row", pairs)
            total = total + jnp.dot(moved, down_blocks[step], preferred_element_type=jnp.float32)
        result = total.astype(jnp.bfloat16)
        result = result.reshape(groups, columns, span, quarter).transpose(1, 0, 2, 3)
        back = lax.all_to_all(result, "col", split_axis=0, concat_axis=0, tiled=True)
        match = (all_slots[:, :, :, None] == wanted.astype(jnp.float32)[None, None, None, :])
        weights = jnp.sum(jnp.where(match, all_shares[:, :, :, None], 0.0), axis=2)
        weights = weights.reshape(groups, token_count, experts, span)
        combined = combined + jnp.einsum(
            "rtep,erpf->rtf", weights, back.astype(jnp.float32),
            precision=lax.Precision.HIGHEST, preferred_element_type=jnp.float32,
        )
    combined = combined.astype(jnp.bfloat16)
    home = lax.all_to_all(combined, "row", split_axis=0, concat_axis=2, tiled=True)
    return home.reshape(token_count, width)


def solution(mesh):
    placed = (
        P(("row", "col"), None),
        P(("row", "col"), None),
        P(("row", "col"), None),
        P("col", None, "row"),
        P("col", None, "row"),
        P("col", None, "row"),
    )
    return jax.shard_map(
        local, mesh=mesh, in_specs=placed, out_specs=P(("row", "col"), None), check_vma=False
    )
```

```python
import jax
import jax.numpy as jnp
from jax import lax
from jax.sharding import PartitionSpec as P

CHUNKS = ((0, 2), (2, 5))


def local(tokens, expert_ids, gate_weights, w_gate, w_up, w_down):
    token_count, top_count = expert_ids.shape
    width = tokens.shape[1]
    unit_count = w_gate.shape[2]
    quarter = w_down.shape[2]
    columns = lax.axis_size("col")
    groups = lax.axis_size("row")
    experts = w_gate.shape[0] * columns
    capacity = max(2, token_count * top_count * 5 // (4 * experts))
    flat_ids = expert_ids.reshape(-1)
    onehot = (flat_ids[:, None] == jnp.arange(experts, dtype=jnp.int32)[None, :]).astype(jnp.int32)
    earlier = jnp.cumsum(onehot, axis=0) - onehot
    position = jnp.sum(earlier * onehot, axis=1)
    slot_ids = (flat_ids * capacity + position).reshape(token_count, top_count)
    shares = gate_weights / jnp.sum(gate_weights, axis=1, keepdims=True)

    meta = jnp.concatenate([slot_ids.astype(jnp.float32), shares], axis=1)
    my_row = lax.axis_index("row")
    shifted = [meta]
    for step in range(1, groups):
        pairs = [(i, (i + step) % groups) for i in range(groups)]
        shifted.append(lax.ppermute(meta, "row", pairs))
    order = jnp.stack([shifted[(-s) % groups] for s in range(groups)])
    meta = jnp.roll(order, my_row, axis=0)

    w_down_parts = w_down[0].reshape(groups, unit_count, quarter)
    combined = jnp.zeros((groups, token_count, quarter), jnp.float32)
    previous = None
    stages = []
    for lo, hi in CHUNKS:
        span = hi - lo
        wanted = (
            jnp.arange(experts, dtype=jnp.int32)[:, None] * capacity
            + jnp.arange(lo, hi, dtype=jnp.int32)[None, :]
        ).reshape(-1)
        chooser = jnp.any(
            wanted[:, None, None] == slot_ids[None, :, :], axis=2
        ).astype(jnp.bfloat16)
        outgoing = jnp.dot(chooser, tokens, preferred_element_type=jnp.float32).astype(jnp.bfloat16)
        outgoing = outgoing.reshape(columns, span * width // 128, 128)
        if previous is not None:
            outgoing, _, meta = lax.optimization_barrier((outgoing, previous, meta))
        arrived = lax.all_to_all(outgoing, "col", split_axis=0, concat_axis=0, tiled=True)
        previous = arrived
        rows = lax.all_gather(arrived, "row", axis=0, tiled=False)
        rows = rows.reshape(groups * columns, span, width // 128, 128)
        gate_w = w_gate[0].reshape(width // 128, 128, unit_count)
        up_w = w_up[0].reshape(width // 128, 128, unit_count)
        gate_part = jnp.einsum("npak,aku->npu", rows, gate_w, preferred_element_type=jnp.float32)
        up_part = jnp.einsum("npak,aku->npu", rows, up_w, preferred_element_type=jnp.float32)
        gate_part = gate_part.reshape(groups * columns * span, unit_count)
        up_part = up_part.reshape(groups * columns * span, unit_count)
        hidden = (jax.nn.silu(gate_part) * up_part).astype(jnp.bfloat16)
        stages.append((span, wanted, hidden))

    all_slots = meta[:, :, :top_count]
    all_shares = meta[:, :, top_count:]
    down_blocks = [
        lax.dynamic_index_in_dim(w_down_parts, (my_row - step) % groups, axis=0, keepdims=False)
        for step in range(groups)
    ]
    combined = jnp.zeros((groups, token_count, quarter), jnp.float32)
    for index, (span, wanted, hidden) in enumerate(stages):
        def down(part, block):
            part = part.reshape(groups, columns, span, unit_count)
            return jnp.einsum("rcpu,uf->crpf", part, block, preferred_element_type=jnp.float32)

        total = down(hidden, down_blocks[0])
        for step in range(1, groups):
            pairs = [(i, (i + step) % groups) for i in range(groups)]
            moved = lax.ppermute(hidden, "row", pairs)
            total = total + down(moved, down_blocks[step])
        result = total.astype(jnp.bfloat16)
        back = lax.all_to_all(result, "col", split_axis=0, concat_axis=0, tiled=True)
        match = (all_slots[:, :, :, None] == wanted.astype(jnp.float32)[None, None, None, :])
        weights = jnp.sum(jnp.where(match, all_shares[:, :, :, None], 0.0), axis=2)
        weights = weights.reshape(groups, token_count, experts, span)
        combined = combined + jnp.einsum(
            "rtep,erpf->rtf", weights, back.astype(jnp.float32),
            precision=lax.Precision.HIGHEST, preferred_element_type=jnp.float32,
        )
    combined = combined.astype(jnp.bfloat16)
    home = lax.all_to_all(combined, "row", split_axis=0, concat_axis=2, tiled=True)
    return home.reshape(token_count, width)


def solution(mesh):
    placed = (
        P(("row", "col"), None),
        P(("row", "col"), None),
        P(("row", "col"), None),
        P("col", None, "row"),
        P("col", None, "row"),
        P("col", None, "row"),
    )
    return jax.shard_map(
        local, mesh=mesh, in_specs=placed, out_specs=P(("row", "col"), None), check_vma=False
    )
```

```python
import jax
import jax.numpy as jnp
from jax import lax
from jax.sharding import PartitionSpec as P

CHUNKS = ((0, 2), (2, 5))


def local(tokens, expert_ids, gate_weights, w_gate, w_up, w_down):
    token_count, top_count = expert_ids.shape
    width = tokens.shape[1]
    unit_count = w_gate.shape[2]
    quarter = w_down.shape[2]
    columns = lax.axis_size("col")
    groups = lax.axis_size("row")
    experts = w_gate.shape[0] * columns
    capacity = max(2, token_count * top_count * 5 // (4 * experts))
    flat_ids = expert_ids.reshape(-1)
    onehot = (flat_ids[:, None] == jnp.arange(experts, dtype=jnp.int32)[None, :]).astype(jnp.int32)
    earlier = jnp.cumsum(onehot, axis=0) - onehot
    position = jnp.sum(earlier * onehot, axis=1)
    slot_ids = (flat_ids * capacity + position).reshape(token_count, top_count)
    shares = gate_weights / jnp.sum(gate_weights, axis=1, keepdims=True)

    meta = jnp.concatenate([slot_ids.astype(jnp.float32), shares], axis=1)
    my_row = lax.axis_index("row")
    shifted = [meta]
    for step in range(1, groups):
        pairs = [(i, (i + step) % groups) for i in range(groups)]
        shifted.append(lax.ppermute(meta, "row", pairs))
    order = jnp.stack([shifted[(-s) % groups] for s in range(groups)])
    meta = jnp.roll(order, my_row, axis=0)

    w_down_parts = w_down[0].reshape(groups, unit_count, quarter)
    combined = jnp.zeros((groups, token_count, quarter), jnp.float32)
    previous = None
    stages = []
    for lo, hi in CHUNKS:
        span = hi - lo
        wanted = (
            jnp.arange(experts, dtype=jnp.int32)[:, None] * capacity
            + jnp.arange(lo, hi, dtype=jnp.int32)[None, :]
        ).reshape(-1)
        chooser = jnp.any(
            wanted[:, None, None] == slot_ids[None, :, :], axis=2
        ).astype(jnp.bfloat16)
        outgoing = jnp.dot(chooser, tokens, preferred_element_type=jnp.float32).astype(jnp.bfloat16)
        outgoing = outgoing.reshape(columns, span * width // 128, 128)
        if previous is not None:
            outgoing, _, meta = lax.optimization_barrier((outgoing, previous, meta))
        arrived = lax.all_to_all(outgoing, "col", split_axis=0, concat_axis=0, tiled=True)
        previous = arrived
        rows = lax.all_gather(arrived, "row", axis=0, tiled=False)
        rows = rows.reshape(groups * columns, span, width // 128, 128)
        gate_w = w_gate[0].reshape(width // 128, 128, unit_count)
        up_w = w_up[0].reshape(width // 128, 128, unit_count)
        gate_part = jnp.einsum("npak,aku->npu", rows, gate_w, preferred_element_type=jnp.float32)
        up_part = jnp.einsum("npak,aku->npu", rows, up_w, preferred_element_type=jnp.float32)
        gate_part = gate_part.reshape(groups * columns * span, unit_count)
        up_part = up_part.reshape(groups * columns * span, unit_count)
        hidden = (jax.nn.silu(gate_part) * up_part).astype(jnp.bfloat16)
        stages.append((span, wanted, hidden))

    all_slots = meta[:, :, :top_count]
    all_shares = meta[:, :, top_count:]
    down_blocks = [
        lax.dynamic_index_in_dim(w_down_parts, (my_row - step) % groups, axis=0, keepdims=False)
        for step in range(groups)
    ]
    combined = jnp.zeros((groups, token_count, quarter), jnp.float32)
    for index, (span, wanted, hidden) in enumerate(stages):
        total = jnp.dot(hidden, down_blocks[0], preferred_element_type=jnp.float32)
        for step in range(1, groups):
            pairs = [(i, (i + step) % groups) for i in range(groups)]
            moved = lax.ppermute(hidden, "row", pairs)
            total = total + jnp.dot(moved, down_blocks[step], preferred_element_type=jnp.float32)
        result = total.astype(jnp.bfloat16)
        result = result.reshape(groups, columns, span, quarter).transpose(1, 0, 2, 3)
        back = lax.all_to_all(result, "col", split_axis=0, concat_axis=0, tiled=True)
        match = (all_slots[:, :, :, None] == wanted.astype(jnp.float32)[None, None, None, :])
        weights = jnp.sum(jnp.where(match, all_shares[:, :, :, None], 0.0), axis=2)
        weights = weights.reshape(groups, token_count, experts, span)
        combined = combined + jnp.einsum(
            "rtep,erpf->rtf", weights, back.astype(jnp.float32),
            precision=lax.Precision.HIGHEST, preferred_element_type=jnp.float32,
        )
        if index + 1 < len(stages):
            combined, later = lax.optimization_barrier((combined, stages[index + 1][2]))
            stages[index + 1] = stages[index + 1][:2] + (later,)
    combined = combined.astype(jnp.bfloat16)
    home = lax.all_to_all(combined.transpose(1, 0, 2), "row", split_axis=1, concat_axis=1, tiled=True)
    return home.reshape(token_count, width)


def solution(mesh):
    placed = (
        P(("row", "col"), None),
        P(("row", "col"), None),
        P(("row", "col"), None),
        P("col", None, "row"),
        P("col", None, "row"),
        P("col", None, "row"),
    )
    return jax.shard_map(
        local, mesh=mesh, in_specs=placed, out_specs=P(("row", "col"), None), check_vma=False
    )
```

```python
import jax
import jax.numpy as jnp
from jax import lax
from jax.sharding import Mesh, PartitionSpec as P

CHUNKS = ((0, 2), (2, 5))


def local(tokens, expert_ids, gate_weights, w_gate, w_up, w_down):
    token_count, top_count = expert_ids.shape
    width = tokens.shape[1]
    unit_count = w_gate.shape[2]
    quarter = w_down.shape[2]
    high = lax.axis_size("hi")
    low = lax.axis_size("lo")
    columns = high * low
    groups = lax.axis_size("row")
    experts = w_gate.shape[0] * columns
    capacity = max(2, token_count * top_count * 5 // (4 * experts))
    flat_ids = expert_ids.reshape(-1)
    onehot = (flat_ids[:, None] == jnp.arange(experts, dtype=jnp.int32)[None, :]).astype(jnp.int32)
    earlier = jnp.cumsum(onehot, axis=0) - onehot
    position = jnp.sum(earlier * onehot, axis=1)
    slot_ids = (flat_ids * capacity + position).reshape(token_count, top_count)
    shares = gate_weights / jnp.sum(gate_weights, axis=1, keepdims=True)

    meta = jnp.concatenate([slot_ids.astype(jnp.float32), shares], axis=1)
    my_row = lax.axis_index("row")
    shifted = [meta]
    for step in range(1, groups):
        pairs = [(i, (i + step) % groups) for i in range(groups)]
        shifted.append(lax.ppermute(meta, "row", pairs))
    order = jnp.stack([shifted[(-s) % groups] for s in range(groups)])
    meta = jnp.roll(order, my_row, axis=0)

    w_down_parts = w_down[0].reshape(groups, unit_count, quarter)
    combined = jnp.zeros((groups, token_count, quarter), jnp.float32)
    previous = None
    stages = []
    for lo, hi in CHUNKS:
        span = hi - lo
        wanted = (
            jnp.arange(experts, dtype=jnp.int32)[:, None] * capacity
            + jnp.arange(lo, hi, dtype=jnp.int32)[None, :]
        ).reshape(-1)
        chooser = jnp.any(
            wanted[:, None, None] == slot_ids[None, :, :], axis=2
        ).astype(jnp.bfloat16)
        outgoing = jnp.dot(chooser, tokens, preferred_element_type=jnp.float32).astype(jnp.bfloat16)
        outgoing = outgoing.reshape(columns, span * width // 128, 128)
        if previous is not None:
            outgoing, _, meta = lax.optimization_barrier((outgoing, previous, meta))
        staged = outgoing.reshape(high, low, span * width // 128, 128)
        staged = lax.all_to_all(staged, "lo", split_axis=1, concat_axis=1, tiled=True)
        staged = lax.all_to_all(staged, "hi", split_axis=0, concat_axis=0, tiled=True)
        arrived = staged.reshape(columns, span * width // 128, 128)
        previous = arrived
        rows = lax.all_gather(arrived, "row", axis=0, tiled=False)
        rows = rows.reshape(groups * columns, span, width // 128, 128)
        gate_w = w_gate[0].reshape(width // 128, 128, unit_count)
        up_w = w_up[0].reshape(width // 128, 128, unit_count)
        gate_part = jnp.einsum("npak,aku->npu", rows, gate_w, preferred_element_type=jnp.float32)
        up_part = jnp.einsum("npak,aku->npu", rows, up_w, preferred_element_type=jnp.float32)
        gate_part = gate_part.reshape(groups * columns * span, unit_count)
        up_part = up_part.reshape(groups * columns * span, unit_count)
        hidden = (jax.nn.silu(gate_part) * up_part).astype(jnp.bfloat16)
        stages.append((span, wanted, hidden))

    all_slots = meta[:, :, :top_count]
    all_shares = meta[:, :, top_count:]
    down_blocks = [
        lax.dynamic_index_in_dim(w_down_parts, (my_row - step) % groups, axis=0, keepdims=False)
        for step in range(groups)
    ]
    combined = jnp.zeros((groups, token_count, quarter), jnp.float32)
    for index, (span, wanted, hidden) in enumerate(stages):
        total = jnp.dot(hidden, down_blocks[0], preferred_element_type=jnp.float32)
        for step in range(1, groups):
            pairs = [(i, (i + step) % groups) for i in range(groups)]
            moved = lax.ppermute(hidden, "row", pairs)
            total = total + jnp.dot(moved, down_blocks[step], preferred_element_type=jnp.float32)
        result = total.astype(jnp.bfloat16)
        result = result.reshape(groups, columns, span, quarter).transpose(1, 0, 2, 3)
        back = lax.all_to_all(result, ("hi", "lo"), split_axis=0, concat_axis=0, tiled=True)
        match = (all_slots[:, :, :, None] == wanted.astype(jnp.float32)[None, None, None, :])
        weights = jnp.sum(jnp.where(match, all_shares[:, :, :, None], 0.0), axis=2)
        weights = weights.reshape(groups, token_count, experts, span)
        combined = combined + jnp.einsum(
            "rtep,erpf->rtf", weights, back.astype(jnp.float32),
            precision=lax.Precision.HIGHEST, preferred_element_type=jnp.float32,
        )
    combined = combined.astype(jnp.bfloat16)
    home = lax.all_to_all(combined, "row", split_axis=0, concat_axis=2, tiled=True)
    return home.reshape(token_count, width)


def solution(mesh):
    high = mesh.devices.shape[1] // 8 if mesh.devices.shape[1] % 8 == 0 else 1
    split = Mesh(
        mesh.devices.reshape(mesh.devices.shape[0], high, mesh.devices.shape[1] // high),
        ("row", "hi", "lo"),
    )
    tokens_spec = P(("row", "hi", "lo"), None)
    weights_spec = P(("hi", "lo"), None, "row")
    placed = (tokens_spec, tokens_spec, tokens_spec, weights_spec, weights_spec, weights_spec)
    return jax.shard_map(
        local, mesh=split, in_specs=placed, out_specs=tokens_spec, check_vma=False
    )
```

```python
import jax
import jax.numpy as jnp
from jax import lax
from jax.sharding import PartitionSpec as P

CHUNKS = ((0, 2), (2, 5))


def local(tokens, expert_ids, gate_weights, w_gate, w_up, w_down):
    token_count, top_count = expert_ids.shape
    width = tokens.shape[1]
    unit_count = w_gate.shape[2]
    quarter = w_down.shape[2]
    columns = lax.axis_size("col")
    groups = lax.axis_size("row")
    experts = w_gate.shape[0] * columns
    capacity = max(2, token_count * top_count * 5 // (4 * experts))
    flat_ids = expert_ids.reshape(-1)
    onehot = (flat_ids[:, None] == jnp.arange(experts, dtype=jnp.int32)[None, :]).astype(jnp.int32)
    earlier = jnp.cumsum(onehot, axis=0) - onehot
    position = jnp.sum(earlier * onehot, axis=1)
    slot_ids = (flat_ids * capacity + position).reshape(token_count, top_count)
    shares = gate_weights / jnp.sum(gate_weights, axis=1, keepdims=True)

    meta = jnp.concatenate([slot_ids.astype(jnp.float32), shares], axis=1)
    my_row = lax.axis_index("row")
    shifted = [meta]
    for step in range(1, groups):
        pairs = [(i, (i + step) % groups) for i in range(groups)]
        shifted.append(lax.ppermute(meta, "row", pairs))
    order = jnp.stack([shifted[(-s) % groups] for s in range(groups)])
    meta = jnp.roll(order, my_row, axis=0)

    w_down_parts = w_down[0].reshape(groups, unit_count, quarter)
    combined = jnp.zeros((groups, token_count, quarter), jnp.float32)
    previous = None
    stages = []
    for lo, hi in CHUNKS:
        span = hi - lo
        wanted = (
            jnp.arange(experts, dtype=jnp.int32)[:, None] * capacity
            + jnp.arange(lo, hi, dtype=jnp.int32)[None, :]
        ).reshape(-1)
        chooser = jnp.any(
            wanted[:, None, None] == slot_ids[None, :, :], axis=2
        ).astype(jnp.bfloat16)
        outgoing = jnp.dot(chooser, tokens, preferred_element_type=jnp.float32).astype(jnp.bfloat16)
        outgoing = outgoing.reshape(columns, span * width // 128, 128)
        if previous is not None:
            outgoing, _, meta = lax.optimization_barrier((outgoing, previous, meta))
        arrived = lax.all_to_all(outgoing, "col", split_axis=0, concat_axis=0, tiled=True)
        previous = arrived
        rows = lax.all_gather(arrived, "row", axis=0, tiled=False)
        rows = rows.reshape(groups * columns, span, width // 128, 128)
        gate_w = w_gate[0].reshape(width // 128, 128, unit_count)
        up_w = w_up[0].reshape(width // 128, 128, unit_count)
        gate_part = jnp.einsum("npak,aku->npu", rows, gate_w, preferred_element_type=jnp.float32)
        up_part = jnp.einsum("npak,aku->npu", rows, up_w, preferred_element_type=jnp.float32)
        gate_part = gate_part.reshape(groups * columns * span, unit_count)
        up_part = up_part.reshape(groups * columns * span, unit_count)
        hidden = (jax.nn.silu(gate_part) * up_part).astype(jnp.bfloat16)
        stages.append((span, wanted, hidden))

    all_slots = meta[:, :, :top_count]
    all_shares = meta[:, :, top_count:]
    down_blocks = [
        lax.dynamic_index_in_dim(w_down_parts, (my_row - step) % groups, axis=0, keepdims=False)
        for step in range(groups)
    ]
    combined = jnp.zeros((groups, token_count, quarter), jnp.float32)
    for index, (span, wanted, hidden) in enumerate(stages):
        earlier_done = index > 0
        total = jnp.dot(hidden, down_blocks[0], preferred_element_type=jnp.float32)
        for step in range(1, groups):
            pairs = [(i, (i + step) % groups) for i in range(groups)]
            moved = lax.ppermute(hidden, "row", pairs)
            total = total + jnp.dot(moved, down_blocks[step], preferred_element_type=jnp.float32)
        result = total.astype(jnp.bfloat16)
        result = result.reshape(groups, columns, span, quarter).transpose(1, 0, 2, 3)
        if earlier_done:
            result, combined = lax.optimization_barrier((result, combined))
        back = lax.all_to_all(result, "col", split_axis=0, concat_axis=0, tiled=True)
        match = (all_slots[:, :, :, None] == wanted.astype(jnp.float32)[None, None, None, :])
        weights = jnp.sum(jnp.where(match, all_shares[:, :, :, None], 0.0), axis=2)
        weights = weights.reshape(groups, token_count, experts, span)
        combined = combined + jnp.einsum(
            "rtep,erpf->rtf", weights, back.astype(jnp.float32),
            precision=lax.Precision.HIGHEST, preferred_element_type=jnp.float32,
        )
    combined = combined.astype(jnp.bfloat16)
    home = lax.all_to_all(combined, "row", split_axis=0, concat_axis=2, tiled=True)
    return home.reshape(token_count, width)


def solution(mesh):
    placed = (
        P(("row", "col"), None),
        P(("row", "col"), None),
        P(("row", "col"), None),
        P("col", None, "row"),
        P("col", None, "row"),
        P("col", None, "row"),
    )
    return jax.shard_map(
        local, mesh=mesh, in_specs=placed, out_specs=P(("row", "col"), None), check_vma=False
    )
```

```python
import jax
import jax.numpy as jnp
from jax import lax
from jax.sharding import PartitionSpec as P

CHUNKS = ((0, 2), (2, 5))


def local(tokens, expert_ids, gate_weights, w_gate, w_up, w_down):
    token_count, top_count = expert_ids.shape
    width = tokens.shape[1]
    unit_count = w_gate.shape[2]
    quarter = w_down.shape[2]
    columns = lax.axis_size("col")
    groups = lax.axis_size("row")
    experts = w_gate.shape[0] * columns
    capacity = max(2, token_count * top_count * 5 // (4 * experts))
    flat_ids = expert_ids.reshape(-1)
    onehot = (flat_ids[:, None] == jnp.arange(experts, dtype=jnp.int32)[None, :]).astype(jnp.int32)
    earlier = jnp.cumsum(onehot, axis=0) - onehot
    position = jnp.sum(earlier * onehot, axis=1)
    slot_ids = (flat_ids * capacity + position).reshape(token_count, top_count)
    shares = gate_weights / jnp.sum(gate_weights, axis=1, keepdims=True)

    meta = jnp.concatenate([slot_ids.astype(jnp.float32), shares], axis=1)
    my_row = lax.axis_index("row")
    shifted = [meta]
    for step in range(1, groups):
        pairs = [(i, (i + step) % groups) for i in range(groups)]
        shifted.append(lax.ppermute(meta, "row", pairs))
    order = jnp.stack([shifted[(-s) % groups] for s in range(groups)])
    meta = jnp.roll(order, my_row, axis=0)

    w_down_parts = w_down[0].reshape(groups, unit_count, quarter)
    combined = jnp.zeros((groups, token_count, quarter), jnp.float32)
    previous = None
    stages = []
    for lo, hi in CHUNKS:
        span = hi - lo
        wanted = (
            jnp.arange(experts, dtype=jnp.int32)[:, None] * capacity
            + jnp.arange(lo, hi, dtype=jnp.int32)[None, :]
        ).reshape(-1)
        chooser = jnp.any(
            wanted[:, None, None] == slot_ids[None, :, :], axis=2
        ).astype(jnp.bfloat16)
        outgoing = jnp.dot(chooser, tokens, preferred_element_type=jnp.float32).astype(jnp.bfloat16)
        outgoing = outgoing.reshape(columns, span * width // 128, 128)
        if previous is not None:
            outgoing, _, meta = lax.optimization_barrier((outgoing, previous, meta))
        arrived = lax.all_to_all(outgoing, "col", split_axis=0, concat_axis=0, tiled=True)
        previous = arrived
        rows = lax.all_gather(arrived, "row", axis=0, tiled=False)
        rows = rows.reshape(groups * columns, span, width // 128, 128)
        gate_w = w_gate[0].reshape(width // 128, 128, unit_count)
        up_w = w_up[0].reshape(width // 128, 128, unit_count)
        gate_part = jnp.einsum("npak,aku->npu", rows, gate_w, preferred_element_type=jnp.float32)
        up_part = jnp.einsum("npak,aku->npu", rows, up_w, preferred_element_type=jnp.float32)
        gate_part = gate_part.reshape(groups * columns * span, unit_count)
        up_part = up_part.reshape(groups * columns * span, unit_count)
        hidden = (jax.nn.silu(gate_part) * up_part).astype(jnp.bfloat16)
        stages.append((span, wanted, hidden))

    all_slots = meta[:, :, :top_count]
    all_shares = meta[:, :, top_count:]
    down_blocks = [
        lax.dynamic_index_in_dim(w_down_parts, (my_row - step) % groups, axis=0, keepdims=False)
        for step in range(groups)
    ]
    combined = jnp.zeros((groups, token_count, quarter), jnp.float32)
    for index, (span, wanted, hidden) in enumerate(stages):
        total = jnp.dot(hidden, down_blocks[0], preferred_element_type=jnp.float32)
        for step in range(1, groups):
            pairs = [(i, (i + step) % groups) for i in range(groups)]
            moved = lax.ppermute(hidden, "row", pairs)
            total = total + jnp.dot(moved, down_blocks[step], preferred_element_type=jnp.float32)
        result = total.astype(jnp.bfloat16)
        result = result.reshape(groups, columns, span, quarter).transpose(1, 0, 2, 3)
        back = lax.all_to_all(result, "col", split_axis=0, concat_axis=0, tiled=True)
        match = (all_slots[:, :, :, None] == wanted.astype(jnp.float32)[None, None, None, :])
        weights = jnp.sum(jnp.where(match, all_shares[:, :, :, None], 0.0), axis=2)
        weights = weights.reshape(groups, token_count, experts, span)
        combined = combined + jnp.einsum(
            "rtep,erpf->rtf", weights, back.astype(jnp.float32),
            precision=lax.Precision.HIGHEST, preferred_element_type=jnp.float32,
        )
    combined = combined.astype(jnp.bfloat16)
    home = lax.all_to_all(combined, "row", split_axis=0, concat_axis=0, tiled=True)
    return jnp.concatenate([home[j] for j in range(groups)], axis=1)


def solution(mesh):
    placed = (
        P(("row", "col"), None),
        P(("row", "col"), None),
        P(("row", "col"), None),
        P("col", None, "row"),
        P("col", None, "row"),
        P("col", None, "row"),
    )
    return jax.shard_map(
        local, mesh=mesh, in_specs=placed, out_specs=P(("row", "col"), None), check_vma=False
    )
```

```python
import jax
import jax.numpy as jnp
from jax import lax
from jax.sharding import PartitionSpec as P

CHUNKS = ((0, 2), (2, 5))


def local(tokens, expert_ids, gate_weights, w_gate, w_up, w_down):
    token_count, top_count = expert_ids.shape
    width = tokens.shape[1]
    unit_count = w_gate.shape[2]
    quarter = w_down.shape[2]
    columns = lax.axis_size("col")
    groups = lax.axis_size("row")
    experts = w_gate.shape[0] * columns
    capacity = max(2, token_count * top_count * 5 // (4 * experts))
    flat_ids = expert_ids.reshape(-1)
    onehot = (flat_ids[:, None] == jnp.arange(experts, dtype=jnp.int32)[None, :]).astype(jnp.int32)
    earlier = jnp.cumsum(onehot, axis=0) - onehot
    position = jnp.sum(earlier * onehot, axis=1)
    slot_ids = (flat_ids * capacity + position).reshape(token_count, top_count)
    shares = gate_weights / jnp.sum(gate_weights, axis=1, keepdims=True)

    meta = jnp.concatenate([slot_ids.astype(jnp.float32), shares], axis=1)
    my_row = lax.axis_index("row")
    shifted = [meta]
    for step in range(1, groups):
        pairs = [(i, (i + step) % groups) for i in range(groups)]
        shifted.append(lax.ppermute(meta, "row", pairs))
    order = jnp.stack([shifted[(-s) % groups] for s in range(groups)])
    meta = jnp.roll(order, my_row, axis=0)

    w_down_parts = w_down[0].reshape(groups, unit_count, quarter)
    combined = jnp.zeros((groups, token_count, quarter), jnp.float32)
    previous = None
    stages = []
    for lo, hi in CHUNKS:
        span = hi - lo
        wanted = (
            jnp.arange(experts, dtype=jnp.int32)[:, None] * capacity
            + jnp.arange(lo, hi, dtype=jnp.int32)[None, :]
        ).reshape(-1)
        chooser = jnp.any(
            wanted[:, None, None] == slot_ids[None, :, :], axis=2
        ).astype(jnp.bfloat16)
        outgoing = jnp.dot(chooser, tokens, preferred_element_type=jnp.float32).astype(jnp.bfloat16)
        outgoing = outgoing.reshape(columns, span * width // 128, 128)
        if previous is not None:
            outgoing, _, meta = lax.optimization_barrier((outgoing, previous, meta))
        arrived = lax.all_to_all(outgoing, "col", split_axis=0, concat_axis=0, tiled=True)
        previous = arrived
        rows = lax.all_gather(arrived, "row", axis=0, tiled=False)
        rows = rows.reshape(groups * columns, span, width // 128, 128)
        gate_w = w_gate[0].reshape(width // 128, 128, unit_count)
        up_w = w_up[0].reshape(width // 128, 128, unit_count)
        gate_part = jnp.einsum("npak,aku->npu", rows, gate_w, preferred_element_type=jnp.float32)
        up_part = jnp.einsum("npak,aku->npu", rows, up_w, preferred_element_type=jnp.float32)
        gate_part = gate_part.reshape(groups * columns * span, unit_count)
        up_part = up_part.reshape(groups * columns * span, unit_count)
        hidden = (jax.nn.silu(gate_part) * up_part).astype(jnp.bfloat16)
        stages.append((span, wanted, hidden))

    all_slots = meta[:, :, :top_count]
    all_shares = meta[:, :, top_count:]
    down_blocks = [
        lax.dynamic_index_in_dim(w_down_parts, (my_row - step) % groups, axis=0, keepdims=False)
        for step in range(groups)
    ]
    combined = jnp.zeros((groups, token_count, quarter), jnp.float32)
    for index, (span, wanted, hidden) in enumerate(stages):
        total = jnp.dot(hidden, down_blocks[0], preferred_element_type=jnp.float32)
        for step in range(1, groups):
            pairs = [(i, (i + step) % groups) for i in range(groups)]
            moved = lax.ppermute(hidden, "row", pairs)
            total = total + jnp.dot(moved, down_blocks[step], preferred_element_type=jnp.float32)
        result = total.astype(jnp.bfloat16)
        result = result.reshape(groups, columns, span, quarter).transpose(1, 0, 2, 3)
        back = lax.all_to_all(result, "col", split_axis=0, concat_axis=0, tiled=True)
        match = (all_slots[:, :, :, None] == wanted.astype(jnp.float32)[None, None, None, :])
        weights = jnp.sum(jnp.where(match, all_shares[:, :, :, None], 0.0), axis=2)
        weights = weights.reshape(groups, token_count, experts, span)
        combined = combined + jnp.einsum(
            "rtep,erpf->rtf", weights, back.astype(jnp.float32),
            precision=lax.Precision.HIGH, preferred_element_type=jnp.float32,
        )
    combined = combined.astype(jnp.bfloat16)
    home = lax.all_to_all(combined, "row", split_axis=0, concat_axis=0, tiled=True)
    return jnp.concatenate([home[j] for j in range(groups)], axis=1)


def solution(mesh):
    placed = (
        P(("row", "col"), None),
        P(("row", "col"), None),
        P(("row", "col"), None),
        P("col", None, "row"),
        P("col", None, "row"),
        P("col", None, "row"),
    )
    return jax.shard_map(
        local, mesh=mesh, in_specs=placed, out_specs=P(("row", "col"), None), check_vma=False
    )
```
